1024 devices in a mesh: grid: 16 (over z_lo, core), patch: 32 (over x, y), cross: 2 (over z_hi).
Axes of the slice: x: 4, y: 8, z: 16 (z_hi: 2, z_lo: 8; z = z_hi * 8 + z_lo), core: 2. Of those that a mesh axis runs over, the one named last changes fastest.
Arguments:
- adjoint_now: float32 [3, 16, 256, 16, 128], P(None, 'grid', 'patch', 'cross'), may hold values from -6 to 6
- adjoint_prev: float32 [3, 16, 256, 16, 128], P(None, 'grid', 'patch', 'cross'), may hold values from -6 to 6
- stiffness: float32 [16, 256, 16, 128], P('grid', 'patch', 'cross'), may hold values from 0.08 to 0.3
- adjoint_source: bfloat16 [2, 3, 16, 256, 16, 128], P(None, None, 'grid', 'patch', 'cross'), may hold values from -6 to 6
- forward_field: bfloat16 [2, 3, 16, 256, 16, 128], P(None, None, 'grid', 'patch', 'cross'), may hold values from -6 to 6
- material_mask: int32 [16, 32, 2], P('grid', 'patch', 'cross'), may hold values 0 or 1
- interface_map: int32 [16, 256, 16], P('grid', 'patch', 'cross'), may hold values from 0 to 63, as said below
Outputs:
- adjoint_final: float32 [3, 16, 256, 16, 128], P(None, 'grid', 'patch', 'cross')
- kernel: float32 [16, 256, 16, 128], P('grid', 'patch', 'cross')
The draws below stay inside these ranges and needn't reach their ends.
Inputs may be any that keep to these rules, and one draw needn't show every extreme that they name: `interface_map`: each value indexes a column of the same patch's plane of 8 x 8 cells, row-major, at most one cell away from the cell's own position along each horizontal dimension; the first and last cells of each patch are fed by their own column.
All inputs are finite; a program needn't handle non-finite values. No bound on the sum of `material_mask` on one device may be relied on, other than what follows from the above.
Results may differ from the reference program's by a relative error of at most 0.00035.
Values sent between devices are 32-bit elements; how exact they have to be, the bound alone decides.
No kernel may reach another device: no remote copies, remote signals or barrier semaphores. Data moves between devices by JAX's collectives and lax.ppermute only.
A program may use at most 32 MiB of HBM per device.

```python
import math
import jax
import jax.numpy as jnp

CX = 8
CY = 8
CZ = 128
STEPS = 2
GRIDS = 16
PATCHES = 32
CROSSES = 2
PX = 256
PY = 16


def draw_interface_map(key, part):
    first_key = jax.random.fold_in(key, 11)
    second_key = jax.random.fold_in(key, 12)
    step_rows = jax.random.randint(first_key, (GRIDS, PX, PY), -1, 2)
    step_cols = jax.random.randint(second_key, (GRIDS, PX, PY), -1, 2)
    local_rows = (jnp.arange(PX, dtype=jnp.int32) % CX)[None, :, None]
    local_cols = (jnp.arange(PY, dtype=jnp.int32) % CY)[None, None, :]
    moved_rows = jnp.clip(local_rows + step_rows, 0, CX - 1)
    moved_cols = jnp.clip(local_cols + step_cols, 0, CY - 1)
    corner = (local_rows == 0) & (local_cols == 0) | (local_rows == CX - 1) & (local_cols == CY - 1)
    final_rows = jnp.where(corner, local_rows, moved_rows)
    final_cols = jnp.where(corner, local_cols, moved_cols)
    return (final_rows * CY + final_cols).astype(jnp.int32)


def touch_ends(values, rng, smallest, high):
    dims = values.shape
    spot = [jax.random.randint(jax.random.fold_in(rng, axis), (), 0, dims[axis]) for axis in range(len(dims))]
    values = values.at[tuple(spot)].set(smallest)
    longest = dims.index(max(dims))
    spot[longest] = (spot[longest] + 1) % dims[longest]
    return values.at[tuple(spot)].set(high)


def block_scale(rng, extent, cuts, low, top_value):
    def one(dim, parts):
        steps = jax.random.uniform(jax.random.fold_in(jax.random.fold_in(rng, 6), dim), (parts,), jnp.float32, low / len(cuts), top_value / len(cuts))
        return jnp.repeat(jnp.exp(steps), extent[dim] // parts).reshape((-1,) + (1,) * (len(extent) - dim - 1))

    gain = one(*cuts[0])
    for cut in cuts[1:]:
        gain = gain * one(*cut)
    return gain


def bell_draw(own_key, shape, spread, most, shards=(), kind=jnp.bfloat16):
    array = spread * jax.random.normal(own_key, shape, jnp.float32)
    if shards:
        array = array * block_scale(own_key, shape, shards, -0.22, 0.18)
    return jnp.clip(array, -most, most).astype(kind)


def setup_inputs(seed: int = 0) -> dict:
    key_of = jax.random.split(jax.random.key(seed), 8)
    adjoint_now = bell_draw(key_of[0], (3, GRIDS, PX, PY, CZ), 1.0, 6.0, ((1, 16), (2, 32), (3, 2)), jnp.float32)
    adjoint_prev = bell_draw(key_of[1], (3, GRIDS, PX, PY, CZ), 1.0, 6.0, ((1, 16), (2, 32), (3, 2)), jnp.float32)
    stiffness = jnp.clip(jnp.exp(math.log(0.3) - 1.3217559 * jax.random.uniform(key_of[2], (GRIDS, PX, PY, CZ), jnp.float32) ** block_scale(key_of[2], (GRIDS, PX, PY, CZ), ((0, 16), (1, 32), (2, 2)), -0.2, 0.2)), 0.08, 0.3)
    adjoint_source = bell_draw(key_of[3], (STEPS, 3, GRIDS, PX, PY, CZ), 1.0, 6.0, ((2, 16), (3, 32), (4, 2)))
    forward_field = bell_draw(key_of[4], (STEPS, 3, GRIDS, PX, PY, CZ), 1.0, 6.0, ((2, 16), (3, 32), (4, 2)))
    material_mask = touch_ends((jax.random.randint(key_of[5], (GRIDS, PATCHES, CROSSES), 0, 4) < 3).astype(jnp.int32), jax.random.fold_in(key_of[5], 1), 0, 1)
    interface_map = draw_interface_map(jax.random.fold_in(key_of[7], 71), 0)
    return dict(adjoint_now=adjoint_now, adjoint_prev=adjoint_prev, stiffness=stiffness, adjoint_source=adjoint_source, forward_field=forward_field, material_mask=material_mask, interface_map=interface_map)


def lap_field(field, material_rows, material_cols, grid_ids):
    bottom = field[:, :, :, :, -1]
    above = jnp.concatenate([jnp.zeros_like(bottom[:, :1]), bottom[:, :-1]], axis=1)
    mapped = above[:, grid_ids, material_rows, material_cols]
    top_plane = jnp.where(grid_ids == 0, field[:, :, :, :, 0], mapped)
    first = field[:, :, :, :, 0]
    below_plane = jnp.concatenate([first[:, 1:], jnp.zeros_like(first[:, :1])], axis=1)
    upper = jnp.concatenate([top_plane[..., None], field[..., :-1]], axis=4)
    lower = jnp.concatenate([field[..., 1:], below_plane[..., None]], axis=4)
    beside = jnp.roll(field, 1, axis=2) + jnp.roll(field, -1, axis=2)
    beside = beside + jnp.roll(field, 1, axis=3) + jnp.roll(field, -1, axis=3)
    return beside + upper + lower - 6.0 * field


def reference(adjoint_now, adjoint_prev, stiffness, adjoint_source, forward_field, material_mask, interface_map):
    grid_count = interface_map.shape[0]
    rows_all = interface_map.shape[1]
    cols_all = interface_map.shape[2]
    base_rows = (jnp.arange(rows_all, dtype=jnp.int32) // CX * CX)[None, :, None]
    base_cols = (jnp.arange(cols_all, dtype=jnp.int32) // CY * CY)[None, None, :]
    row_index = (base_rows + interface_map // CY).astype(jnp.int32)
    col_index = (base_cols + interface_map % CY).astype(jnp.int32)
    grid_ids = jnp.broadcast_to(jnp.arange(grid_count, dtype=jnp.int32)[:, None, None], interface_map.shape)
    cell_mask = jnp.repeat(jnp.repeat(material_mask, CX, axis=1), CY, axis=2).astype(jnp.float32)[:, :, :, None]
    field = adjoint_now
    older = adjoint_prev
    kernel = jnp.zeros(stiffness.shape, jnp.float32)
    for step in range(STEPS):
        slot = STEPS - 1 - step
        lap = lap_field(field, row_index, col_index, grid_ids)
        fresh = (2.0 * field - older + stiffness * lap + adjoint_source[slot].astype(jnp.float32)) * cell_mask
        kernel = kernel + jnp.sum(fresh * forward_field[slot].astype(jnp.float32), axis=0)
        older = field
        field = fresh
    return field, kernel
```

```python
import jax
import jax.numpy as jnp
from jax import lax
from jax.sharding import PartitionSpec as P

STEPS = 2


def ring(axis, by):
    peers = lax.axis_size(axis)
    return [(i, (i + by) % peers) for i in range(peers)]


def open_chain(axis, by):
    peers = lax.axis_size(axis)
    return [(i, i + by) for i in range(peers) if 0 <= i + by < peers]


def exchange(field):
    x_before = lax.ppermute(field[:, :, -1:], "patch", ring("patch", 1))
    x_after = lax.ppermute(field[:, :, :1], "patch", ring("patch", -1))
    peers = lax.axis_size("cross")
    if peers == 1:
        y_before = field[:, :, :, -1:]
        y_after = field[:, :, :, :1]
    elif peers == 2:
        edges = jnp.concatenate([field[:, :, :, :1], field[:, :, :, -1:]], axis=3)
        got = lax.ppermute(edges, "cross", [(0, 1), (1, 0)])
        y_before = got[:, :, :, 1:2]
        y_after = got[:, :, :, 0:1]
    else:
        y_before = lax.ppermute(field[:, :, :, -1:], "cross", ring("cross", 1))
        y_after = lax.ppermute(field[:, :, :, :1], "cross", ring("cross", -1))
    from_above = lax.ppermute(field[:, :, :, :, -1], "grid", open_chain("grid", 1))
    from_below = lax.ppermute(field[:, :, :, :, 0], "grid", open_chain("grid", -1))
    return x_before, x_after, y_before, y_after, from_above, from_below


def local(
    adjoint_now,
    adjoint_prev,
    stiffness,
    adjoint_source,
    forward_field,
    material_mask,
    interface_map,
):
    rows = adjoint_now.shape[2]
    cols = adjoint_now.shape[3]
    flat_map = interface_map.reshape(-1)
    is_top = lax.axis_index("grid") == 0
    patch_mask = material_mask[0, 0, 0].astype(jnp.float32)
    field = adjoint_now
    older = adjoint_prev
    kernel = jnp.zeros(stiffness.shape, jnp.float32)
    for step in range(STEPS):
        slot = STEPS - 1 - step
        x_before, x_after, y_before, y_after, from_above, from_below = exchange(field)
        gathered = jnp.take(from_above.reshape(3, rows * cols), flat_map, axis=1).reshape(
            3, 1, rows, cols
        )
        top_plane = jnp.where(is_top, field[:, :, :, :, 0], gathered)
        upper = jnp.concatenate([top_plane[..., None], field[..., :-1]], axis=4)
        lower = jnp.concatenate([field[..., 1:], from_below[..., None]], axis=4)
        xs = jnp.concatenate([x_before, field, x_after], axis=2)
        ys = jnp.concatenate([y_before, field, y_after], axis=3)
        side = xs[:, :, 2:] + xs[:, :, :-2]
        side = side + ys[:, :, :, 2:] + ys[:, :, :, :-2]
        lap = side + upper + lower - 6.0 * field
        fresh = (
            2.0 * field - older + stiffness * lap + adjoint_source[slot].astype(jnp.float32)
        ) * patch_mask
        kernel = kernel + jnp.sum(fresh * forward_field[slot].astype(jnp.float32), axis=0)
        older = field
        field = fresh
    return (field, kernel)


def solution(mesh):
    in_specs = (
        P(None, "grid", "patch", "cross", None),
        P(None, "grid", "patch", "cross", None),
        P("grid", "patch", "cross", None),
        P(None, None, "grid", "patch", "cross", None),
        P(None, None, "grid", "patch", "cross", None),
        P("grid", "patch", "cross"),
        P("grid", "patch", "cross"),
    )
    out_specs = (P(None, "grid", "patch", "cross", None), P("grid", "patch", "cross", None))
    return jax.shard_map(local, mesh=mesh, in_specs=in_specs, out_specs=out_specs, check_vma=False)
```
